256 devices in a mesh: band: 16 (over z_hi, y, core), grid: 16 (over x, z_lo).
Axes of the slice: x: 4, y: 4, z: 8 (z_hi: 2, z_lo: 4; z = z_hi * 4 + z_lo), core: 2. Of those that a mesh axis runs over, the one named last changes fastest.
Arguments:
- bands: float32 [16, 2, 128, 128, 128], P('band', None, 'grid'), may hold values from -6 to 6
- coulomb: float32 [128, 128, 128], P(None, 'grid'), may hold values from 0.1 to 10
Outputs:
- exchange: float32 [16, 2, 128, 128, 128], P('band', None, 'grid')
The draws below stay inside these ranges and needn't reach their ends.
All inputs are finite; a program needn't handle non-finite values.
Results may differ from the reference program's by a relative error of at most 0.0001.
Values sent between devices are 32-bit elements; how exact they have to be, the bound alone decides.
No kernel may reach another device: no remote copies, remote signals or barrier semaphores. Data moves between devices by JAX's collectives and lax.ppermute only.
A program may use at most 64 MiB of HBM per device.

```python
import math
import jax
import jax.numpy as jnp
from jax import lax

NX = 128
NY = 128
NZ = 128
LOCAL = 1
STEPS = 2
BANDS = 16
N_BAND = 16


def block_levels(rng, extent, shards, least, largest):
    def one(dim, shards_of):
        steps = jax.random.uniform(jax.random.fold_in(jax.random.fold_in(rng, 6), dim), (shards_of,), jnp.float32, least / len(shards), largest / len(shards))
        return jnp.repeat(jnp.exp(steps), extent[dim] // shards_of).reshape((-1,) + (1,) * (len(extent) - dim - 1))

    factor_of = one(*shards[0])
    for cut in shards[1:]:
        factor_of = factor_of * one(*cut)
    return factor_of


def noise(key, dims, scale, reach, split=(), dtype=jnp.bfloat16):
    gain = block_levels(key, dims, split, -0.22, 0.18) if split else 1.0
    values = jax.random.normal(key, dims, jnp.float32) * scale * gain
    return jnp.minimum(jnp.maximum(values, -reach), reach).astype(dtype)


def setup_inputs(seed: int = 0) -> dict:
    key_of = jax.random.split(jax.random.key(seed), 3)
    bands = noise(key_of[0], (BANDS, 2, NX, NY, NZ), 0.7, 6.0, ((0, 16), (2, 16)), jnp.float32)
    coulomb = jnp.clip(jnp.exp(math.log(10.0) - 4.6051702 * jax.random.uniform(key_of[1], (NX, NY, NZ), jnp.float32) ** block_levels(key_of[1], (NX, NY, NZ), ((1, 16),), -0.2, 0.2)), 0.1, 10.0)
    return {"bands": bands, "coulomb": coulomb}


def reference(bands, coulomb):
    wave = lax.complex(bands[:, 0], bands[:, 1])
    pieces = []
    for step_index in range(STEPS):
        owner = (step_index * N_BAND) // STEPS
        pieces.append(wave[owner * LOCAL:(owner + 1) * LOCAL])
    visitors = jnp.concatenate(pieces, axis=0)

    def one_band(orbital):
        total = jnp.zeros_like(orbital)
        for visit_index in range(STEPS * LOCAL):
            partner = visitors[visit_index]
            density = jnp.conj(partner) * orbital
            potential = jnp.fft.ifftn(coulomb * jnp.fft.fftn(density))
            total = total + partner * potential
        return -0.25 * total

    result = lax.map(one_band, wave)
    return jnp.stack([result.real, result.imag], axis=1).astype(jnp.float32)
```

```python
import math

import jax
import jax.numpy as jnp
from jax import lax
from jax.sharding import PartitionSpec as P

NX = 128
NY = 128
NZ = 128
STEPS = 2


einsum_forms = {1: "pnbc,nk->pkbc", 2: "panc,nk->pakc", 3: "pabn,nk->pabk"}


def band_place(half, row, core):
    return half * 8 + row * 2 + core


def half_tree(value, axis):
    def send(operand, pairs):
        return lax.ppermute(operand, axis, [(band_place(h, *a), band_place(h, *b)) for h in (0, 1) for a, b in pairs])

    first = [send(value, [((0, 0), (0, 1))]), send(value, [((0, 0), (1, 0))]), send(value, [((0, 0), (3, 0))])]
    relay = first[1] + first[2]
    second = [
        send(relay, [((1, 0), (1, 1)), ((3, 0), (3, 1))]),
        send(relay, [((1, 0), (2, 0))]),
        send(relay, [((3, 0), (2, 1))]),
    ]
    total = first[0] + relay
    for part in second:
        total = total + part
    return total


def visitors_of(bands, axis):
    index = lax.axis_index(axis)
    head = index % 8 == 0
    own = jnp.where(head, bands, 0).astype(bands.dtype)
    crossed = lax.ppermute(bands, axis, [(0, 8), (8, 0)])
    return [own + half_tree(own, axis), crossed + half_tree(crossed, axis)]


def dft_tables(length):
    indices = jnp.arange(length, dtype=jnp.int32)
    products = indices[:, None] * indices[None, :] % length
    angles = products.astype(jnp.float32) * (2.0 * math.pi / length)
    return (jnp.cos(angles), jnp.sin(angles))


def transform(real_part, imag_part, axis_dim, inverse):
    cosine, sine_table = dft_tables(real_part.shape[axis_dim])
    form = einsum_forms[axis_dim]

    def contract(values, table):
        return jnp.einsum(form, values, table, precision=lax.Precision.HIGHEST)

    re_cos = contract(real_part, cosine)
    re_sin = contract(real_part, sine_table)
    im_cos = contract(imag_part, cosine)
    im_sin = contract(imag_part, sine_table)
    if inverse:
        return (re_cos - im_sin, im_cos + re_sin)
    return (re_cos + im_sin, im_cos - re_sin)


def body(bands, coulomb):
    local = bands.shape[0]
    kernel = coulomb * (1.0 / (NX * NY * NZ))
    own_re = bands[:, 0]
    own_im = bands[:, 1]
    totals = (jnp.zeros_like(own_re), jnp.zeros_like(own_im))
    for visitors in visitors_of(bands, "band"):
        pair_vis_re = visitors[:, 0]
        pair_vis_im = visitors[:, 1]
        pair_real_part = pair_vis_re[None] * own_re[:, None] + pair_vis_im[None] * own_im[:, None]
        pair_imag_part = pair_vis_re[None] * own_im[:, None] - pair_vis_im[None] * own_re[:, None]
        pair_shape = (local * local,) + pair_real_part.shape[2:]
        real_part = pair_real_part.reshape(pair_shape)
        imag_part = pair_imag_part.reshape(pair_shape)
        potentials_real_part = real_part
        potentials_imag_part = imag_part
        potentials_real_part, potentials_imag_part = transform(
            potentials_real_part, potentials_imag_part, 3, False
        )
        potentials_real_part, potentials_imag_part = transform(
            potentials_real_part, potentials_imag_part, 2, False
        )
        stacked = jnp.stack([potentials_real_part, potentials_imag_part], axis=1)
        block = lax.all_to_all(stacked, "grid", split_axis=3, concat_axis=2, tiled=True)
        pencil_real_part, pencil_imag_part = transform(block[:, 0], block[:, 1], 1, False)
        pencil_real_part = pencil_real_part * kernel[None]
        pencil_imag_part = pencil_imag_part * kernel[None]
        pencil_real_part, pencil_imag_part = transform(pencil_real_part, pencil_imag_part, 1, True)
        back = jnp.stack([pencil_real_part, pencil_imag_part], axis=1)
        result = lax.all_to_all(back, "grid", split_axis=2, concat_axis=3, tiled=True)
        potentials_real_part, potentials_imag_part = transform(result[:, 0], result[:, 1], 2, True)
        pot_re, pot_im = transform(potentials_real_part, potentials_imag_part, 3, True)
        accumulate_pot_re = pot_re
        accumulate_pot_im = pot_im
        vis_re = visitors[:, 0][None]
        vis_im = visitors[:, 1][None]
        shape = (local, local) + accumulate_pot_re.shape[1:]
        accumulate_pot_re = accumulate_pot_re.reshape(shape)
        accumulate_pot_im = accumulate_pot_im.reshape(shape)
        add_re = jnp.sum(accumulate_pot_re * vis_re - accumulate_pot_im * vis_im, axis=1)
        add_im = jnp.sum(accumulate_pot_re * vis_im + accumulate_pot_im * vis_re, axis=1)
        totals = (totals[0] + add_re, totals[1] + add_im)
    return -0.25 * jnp.stack([totals[0], totals[1]], axis=1)


def solution(mesh):
    in_specs = (P("band", None, "grid", None, None), P(None, "grid", None))
    out_specs = P("band", None, "grid", None, None)
    return jax.shard_map(body, mesh=mesh, in_specs=in_specs, out_specs=out_specs, check_vma=False)
```

```python
import math

import jax
import jax.numpy as jnp
from jax import lax
from jax.sharding import PartitionSpec as P

NX = 128
NY = 128
NZ = 128
STEPS = 2


einsum_forms = {1: "pnbc,nk->pkbc", 2: "panc,nk->pakc", 3: "pabn,nk->pabk"}


def band_place(half, row, core):
    return half * 8 + row * 2 + core


def half_tree(value, axis):
    def send(operand, pairs):
        return lax.ppermute(operand, axis, [(band_place(h, *a), band_place(h, *b)) for h in (0, 1) for a, b in pairs])

    first = [send(value, [((0, 0), (0, 1))]), send(value, [((0, 0), (1, 0))]), send(value, [((0, 0), (3, 0))])]
    relay = first[1] + first[2]
    second = [
        send(relay, [((1, 0), (1, 1)), ((3, 0), (3, 1))]),
        send(relay, [((1, 0), (2, 0))]),
        send(relay, [((3, 0), (2, 1))]),
    ]
    total = first[0] + relay
    for part in second:
        total = total + part
    return total


def visitors_of(bands, axis):
    index = lax.axis_index(axis)
    head = index % 8 == 0
    own = jnp.where(head, bands, 0).astype(bands.dtype)
    crossed = lax.ppermute(bands, axis, [(0, 8), (8, 0)])
    return [own + half_tree(own, axis), crossed + half_tree(crossed, axis)]


def dft_tables(length):
    indices = jnp.arange(length, dtype=jnp.int32)
    products = indices[:, None] * indices[None, :] % length
    angles = products.astype(jnp.float32) * (2.0 * math.pi / length)
    return (jnp.cos(angles), jnp.sin(angles))


def transform(real_part, imag_part, axis_dim, inverse):
    cosine, sine_table = dft_tables(real_part.shape[axis_dim])
    form = einsum_forms[axis_dim]

    def contract(values, table):
        return jnp.einsum(form, values, table, precision=lax.Precision.HIGHEST)

    re_cos = contract(real_part, cosine)
    re_sin = contract(real_part, sine_table)
    im_cos = contract(imag_part, cosine)
    im_sin = contract(imag_part, sine_table)
    if inverse:
        return (re_cos - im_sin, im_cos + re_sin)
    return (re_cos + im_sin, im_cos - re_sin)


def body(bands, coulomb):
    local = bands.shape[0]
    kernel = coulomb * (1.0 / (NX * NY * NZ))
    own_re = bands[:, 0]
    own_im = bands[:, 1]
    totals = (jnp.zeros_like(own_re), jnp.zeros_like(own_im))
    for visit_index, visitors in enumerate(visitors_of(bands, "band")):
        if visit_index:
            own, visitors = lax.optimization_barrier((bands, visitors))
            own_re = own[:, 0]
            own_im = own[:, 1]
        pair_vis_re = visitors[:, 0]
        pair_vis_im = visitors[:, 1]
        pair_real_part = pair_vis_re[None] * own_re[:, None] + pair_vis_im[None] * own_im[:, None]
        pair_imag_part = pair_vis_re[None] * own_im[:, None] - pair_vis_im[None] * own_re[:, None]
        pair_shape = (local * local,) + pair_real_part.shape[2:]
        real_part = pair_real_part.reshape(pair_shape)
        imag_part = pair_imag_part.reshape(pair_shape)
        potentials_real_part = real_part
        potentials_imag_part = imag_part
        potentials_real_part, potentials_imag_part = transform(
            potentials_real_part, potentials_imag_part, 3, False
        )
        potentials_real_part, potentials_imag_part = transform(
            potentials_real_part, potentials_imag_part, 2, False
        )
        stacked = jnp.stack([potentials_real_part, potentials_imag_part], axis=1)
        block = lax.all_to_all(stacked, "grid", split_axis=3, concat_axis=2, tiled=True)
        pencil_real_part, pencil_imag_part = transform(block[:, 0], block[:, 1], 1, False)
        pencil_real_part = pencil_real_part * kernel[None]
        pencil_imag_part = pencil_imag_part * kernel[None]
        pencil_real_part, pencil_imag_part = transform(pencil_real_part, pencil_imag_part, 1, True)
        back = jnp.stack([pencil_real_part, pencil_imag_part], axis=1)
        result = lax.all_to_all(back, "grid", split_axis=2, concat_axis=3, tiled=True)
        potentials_real_part, potentials_imag_part = transform(result[:, 0], result[:, 1], 2, True)
        pot_re, pot_im = transform(potentials_real_part, potentials_imag_part, 3, True)
        accumulate_pot_re = pot_re
        accumulate_pot_im = pot_im
        vis_re = visitors[:, 0][None]
        vis_im = visitors[:, 1][None]
        shape = (local, local) + accumulate_pot_re.shape[1:]
        accumulate_pot_re = accumulate_pot_re.reshape(shape)
        accumulate_pot_im = accumulate_pot_im.reshape(shape)
        add_re = jnp.sum(accumulate_pot_re * vis_re - accumulate_pot_im * vis_im, axis=1)
        add_im = jnp.sum(accumulate_pot_re * vis_im + accumulate_pot_im * vis_re, axis=1)
        totals = (totals[0] + add_re, totals[1] + add_im)
    return -0.25 * jnp.stack([totals[0], totals[1]], axis=1)


def solution(mesh):
    in_specs = (P("band", None, "grid", None, None), P(None, "grid", None))
    out_specs = P("band", None, "grid", None, None)
    return jax.shard_map(body, mesh=mesh, in_specs=in_specs, out_specs=out_specs, check_vma=False)
```

```python
import math

import jax
import jax.numpy as jnp
from jax import lax
from jax.sharding import PartitionSpec as P

NX = 128
NY = 128
NZ = 128
STEPS = 2


einsum_forms = {1: "pnbc,nk->pkbc", 2: "panc,nk->pakc", 3: "pabn,nk->pabk"}


def band_place(half, row, core):
    return half * 8 + row * 2 + core


def half_tree(value, axis):
    def send(operand, pairs):
        return lax.ppermute(operand, axis, [(band_place(h, *a), band_place(h, *b)) for h in (0, 1) for a, b in pairs])

    first = [send(value, [((0, 0), (0, 1))]), send(value, [((0, 0), (1, 0))]), send(value, [((0, 0), (3, 0))])]
    relay = first[1] + first[2]
    second = [
        send(relay, [((1, 0), (1, 1)), ((3, 0), (3, 1))]),
        send(relay, [((1, 0), (2, 0))]),
        send(relay, [((3, 0), (2, 1))]),
    ]
    total = first[0] + relay
    for part in second:
        total = total + part
    return total


def own_visitor(bands, axis):
    head = lax.axis_index(axis) % 8 == 0
    own = jnp.where(head, bands, 0).astype(bands.dtype)
    return own + half_tree(own, axis)


def crossed_visitor(bands, axis):
    crossed = lax.ppermute(bands, axis, [(0, 8), (8, 0)])
    return crossed + half_tree(crossed, axis)


def dft_tables(length):
    indices = jnp.arange(length, dtype=jnp.int32)
    products = indices[:, None] * indices[None, :] % length
    angles = products.astype(jnp.float32) * (2.0 * math.pi / length)
    return (jnp.cos(angles), jnp.sin(angles))


def transform(real_part, imag_part, axis_dim, inverse):
    cosine, sine_table = dft_tables(real_part.shape[axis_dim])
    form = einsum_forms[axis_dim]

    def contract(values, table):
        return jnp.einsum(form, values, table, precision=lax.Precision.HIGHEST)

    re_cos = contract(real_part, cosine)
    re_sin = contract(real_part, sine_table)
    im_cos = contract(imag_part, cosine)
    im_sin = contract(imag_part, sine_table)
    if inverse:
        return (re_cos - im_sin, im_cos + re_sin)
    return (re_cos + im_sin, im_cos - re_sin)


def body(bands, coulomb):
    local = bands.shape[0]
    kernel = coulomb * (1.0 / (NX * NY * NZ))
    own_re = bands[:, 0]
    own_im = bands[:, 1]
    totals = (jnp.zeros_like(own_re), jnp.zeros_like(own_im))
    gate = None
    for visit_index in range(STEPS):
        if visit_index:
            own, _ = lax.optimization_barrier((bands, gate))
            visitors = crossed_visitor(own, "band")
            own, visitors = lax.optimization_barrier((own, visitors))
            own_re = own[:, 0]
            own_im = own[:, 1]
        else:
            visitors = own_visitor(bands, "band")
        pair_vis_re = visitors[:, 0]
        pair_vis_im = visitors[:, 1]
        pair_real_part = pair_vis_re[None] * own_re[:, None] + pair_vis_im[None] * own_im[:, None]
        pair_imag_part = pair_vis_re[None] * own_im[:, None] - pair_vis_im[None] * own_re[:, None]
        pair_shape = (local * local,) + pair_real_part.shape[2:]
        real_part = pair_real_part.reshape(pair_shape)
        imag_part = pair_imag_part.reshape(pair_shape)
        potentials_real_part = real_part
        potentials_imag_part = imag_part
        potentials_real_part, potentials_imag_part = transform(
            potentials_real_part, potentials_imag_part, 3, False
        )
        potentials_real_part, potentials_imag_part = transform(
            potentials_real_part, potentials_imag_part, 2, False
        )
        stacked = jnp.stack([potentials_real_part, potentials_imag_part], axis=1)
        gate = stacked
        block = lax.all_to_all(stacked, "grid", split_axis=3, concat_axis=2, tiled=True)
        pencil_real_part, pencil_imag_part = transform(block[:, 0], block[:, 1], 1, False)
        pencil_real_part = pencil_real_part * kernel[None]
        pencil_imag_part = pencil_imag_part * kernel[None]
        pencil_real_part, pencil_imag_part = transform(pencil_real_part, pencil_imag_part, 1, True)
        back = jnp.stack([pencil_real_part, pencil_imag_part], axis=1)
        result = lax.all_to_all(back, "grid", split_axis=2, concat_axis=3, tiled=True)
        potentials_real_part, potentials_imag_part = transform(result[:, 0], result[:, 1], 2, True)
        pot_re, pot_im = transform(potentials_real_part, potentials_imag_part, 3, True)
        accumulate_pot_re = pot_re
        accumulate_pot_im = pot_im
        vis_re = visitors[:, 0][None]
        vis_im = visitors[:, 1][None]
        shape = (local, local) + accumulate_pot_re.shape[1:]
        accumulate_pot_re = accumulate_pot_re.reshape(shape)
        accumulate_pot_im = accumulate_pot_im.reshape(shape)
        add_re = jnp.sum(accumulate_pot_re * vis_re - accumulate_pot_im * vis_im, axis=1)
        add_im = jnp.sum(accumulate_pot_re * vis_im + accumulate_pot_im * vis_re, axis=1)
        totals = (totals[0] + add_re, totals[1] + add_im)
    return -0.25 * jnp.stack([totals[0], totals[1]], axis=1)


def solution(mesh):
    in_specs = (P("band", None, "grid", None, None), P(None, "grid", None))
    out_specs = P("band", None, "grid", None, None)
    return jax.shard_map(body, mesh=mesh, in_specs=in_specs, out_specs=out_specs, check_vma=False)
```

```python
import math

import jax
import jax.numpy as jnp
from jax import lax
from jax.sharding import PartitionSpec as P

NX = 128
NY = 128
NZ = 128
STEPS = 2


einsum_forms = {1: "pnbc,nk->pkbc", 2: "panc,nk->pakc", 3: "pabn,nk->pabk"}


def band_place(half, row, core):
    return half * 8 + row * 2 + core


def half_tree(value, axis):
    def send(operand, pairs):
        return lax.ppermute(operand, axis, [(band_place(h, *a), band_place(h, *b)) for h in (0, 1) for a, b in pairs])

    first = [send(value, [((0, 0), (0, 1))]), send(value, [((0, 0), (1, 0))]), send(value, [((0, 0), (3, 0))])]
    relay = first[1] + first[2]
    second = [
        send(relay, [((1, 0), (1, 1)), ((3, 0), (3, 1))]),
        send(relay, [((1, 0), (2, 0))]),
        send(relay, [((3, 0), (2, 1))]),
    ]
    total = first[0] + relay
    for part in second:
        total = total + part
    return total


def swap_with(value, axis, bit):
    return lax.ppermute(value, axis, [(i, i ^ bit) for i in range(16)])


def gathered(mine, axis, bit, low):
    other = swap_with(mine, axis, bit)
    return jnp.where(low, jnp.concatenate([mine, other], axis=2), jnp.concatenate([other, mine], axis=2))


def visitors_of(bands, axis):
    index = lax.axis_index(axis)
    head = index % 8 == 0
    own = jnp.where(head, bands, 0).astype(bands.dtype)
    own = own + half_tree(own, axis)
    place = index % 8
    plane = lax.dynamic_slice_in_dim(own, place * (own.shape[2] // 8), own.shape[2] // 8, axis=2)
    crossed = swap_with(plane, axis, 8)
    for bit in (1, 2, 4):
        crossed = gathered(crossed, axis, bit, index % (2 * bit) < bit)
    return [own, crossed]


def dft_tables(length):
    indices = jnp.arange(length, dtype=jnp.int32)
    products = indices[:, None] * indices[None, :] % length
    angles = products.astype(jnp.float32) * (2.0 * math.pi / length)
    return (jnp.cos(angles), jnp.sin(angles))


def transform(real_part, imag_part, axis_dim, inverse):
    cosine, sine_table = dft_tables(real_part.shape[axis_dim])
    form = einsum_forms[axis_dim]

    def contract(values, table):
        return jnp.einsum(form, values, table, precision=lax.Precision.HIGHEST)

    re_cos = contract(real_part, cosine)
    re_sin = contract(real_part, sine_table)
    im_cos = contract(imag_part, cosine)
    im_sin = contract(imag_part, sine_table)
    if inverse:
        return (re_cos - im_sin, im_cos + re_sin)
    return (re_cos + im_sin, im_cos - re_sin)


def body(bands, coulomb):
    local = bands.shape[0]
    kernel = coulomb * (1.0 / (NX * NY * NZ))
    own_re = bands[:, 0]
    own_im = bands[:, 1]
    totals = (jnp.zeros_like(own_re), jnp.zeros_like(own_im))
    for visit_index, visitors in enumerate(visitors_of(bands, "band")):
        if visit_index:
            own, visitors = lax.optimization_barrier((bands, visitors))
            own_re = own[:, 0]
            own_im = own[:, 1]
        pair_vis_re = visitors[:, 0]
        pair_vis_im = visitors[:, 1]
        pair_real_part = pair_vis_re[None] * own_re[:, None] + pair_vis_im[None] * own_im[:, None]
        pair_imag_part = pair_vis_re[None] * own_im[:, None] - pair_vis_im[None] * own_re[:, None]
        pair_shape = (local * local,) + pair_real_part.shape[2:]
        real_part = pair_real_part.reshape(pair_shape)
        imag_part = pair_imag_part.reshape(pair_shape)
        potentials_real_part = real_part
        potentials_imag_part = imag_part
        potentials_real_part, potentials_imag_part = transform(
            potentials_real_part, potentials_imag_part, 3, False
        )
        potentials_real_part, potentials_imag_part = transform(
            potentials_real_part, potentials_imag_part, 2, False
        )
        stacked = jnp.stack([potentials_real_part, potentials_imag_part], axis=1)
        block = lax.all_to_all(stacked, "grid", split_axis=3, concat_axis=2, tiled=True)
        pencil_real_part, pencil_imag_part = transform(block[:, 0], block[:, 1], 1, False)
        pencil_real_part = pencil_real_part * kernel[None]
        pencil_imag_part = pencil_imag_part * kernel[None]
        pencil_real_part, pencil_imag_part = transform(pencil_real_part, pencil_imag_part, 1, True)
        back = jnp.stack([pencil_real_part, pencil_imag_part], axis=1)
        result = lax.all_to_all(back, "grid", split_axis=2, concat_axis=3, tiled=True)
        potentials_real_part, potentials_imag_part = transform(result[:, 0], result[:, 1], 2, True)
        pot_re, pot_im = transform(potentials_real_part, potentials_imag_part, 3, True)
        accumulate_pot_re = pot_re
        accumulate_pot_im = pot_im
        vis_re = visitors[:, 0][None]
        vis_im = visitors[:, 1][None]
        shape = (local, local) + accumulate_pot_re.shape[1:]
        accumulate_pot_re = accumulate_pot_re.reshape(shape)
        accumulate_pot_im = accumulate_pot_im.reshape(shape)
        add_re = jnp.sum(accumulate_pot_re * vis_re - accumulate_pot_im * vis_im, axis=1)
        add_im = jnp.sum(accumulate_pot_re * vis_im + accumulate_pot_im * vis_re, axis=1)
        totals = (totals[0] + add_re, totals[1] + add_im)
    return -0.25 * jnp.stack([totals[0], totals[1]], axis=1)


def solution(mesh):
    in_specs = (P("band", None, "grid", None, None), P(None, "grid", None))
    out_specs = P("band", None, "grid", None, None)
    return jax.shard_map(body, mesh=mesh, in_specs=in_specs, out_specs=out_specs, check_vma=False)
```

```python
import math

import jax
import jax.numpy as jnp
from jax import lax
from jax.sharding import PartitionSpec as P

NX = 128
NY = 128
NZ = 128
STEPS = 2


einsum_forms = {1: "pnbc,nk->pkbc", 2: "panc,nk->pakc", 3: "pabn,nk->pabk"}


def band_place(half, row, core):
    return half * 8 + row * 2 + core


def half_tree(value, axis):
    def send(operand, pairs):
        return lax.ppermute(operand, axis, [(band_place(h, *a), band_place(h, *b)) for h in (0, 1) for a, b in pairs])

    first = [send(value, [((0, 0), (0, 1))]), send(value, [((0, 0), (1, 0))]), send(value, [((0, 0), (3, 0))])]
    relay = first[1] + first[2]
    second = [
        send(relay, [((1, 0), (1, 1)), ((3, 0), (3, 1))]),
        send(relay, [((1, 0), (2, 0))]),
        send(relay, [((3, 0), (2, 1))]),
    ]
    total = first[0] + relay
    for part in second:
        total = total + part
    return total


def own_visitor(bands, axis):
    head = lax.axis_index(axis) % 8 == 0
    own = jnp.where(head, bands, 0).astype(bands.dtype)
    return own + half_tree(own, axis)


def dft_tables(length):
    indices = jnp.arange(length, dtype=jnp.int32)
    products = indices[:, None] * indices[None, :] % length
    angles = products.astype(jnp.float32) * (2.0 * math.pi / length)
    return (jnp.cos(angles), jnp.sin(angles))


def transform(real_part, imag_part, axis_dim, inverse):
    cosine, sine_table = dft_tables(real_part.shape[axis_dim])
    form = einsum_forms[axis_dim]

    def contract(values, table):
        return jnp.einsum(form, values, table, precision=lax.Precision.HIGHEST)

    re_cos = contract(real_part, cosine)
    re_sin = contract(real_part, sine_table)
    im_cos = contract(imag_part, cosine)
    im_sin = contract(imag_part, sine_table)
    if inverse:
        return (re_cos - im_sin, im_cos + re_sin)
    return (re_cos + im_sin, im_cos - re_sin)


def body(bands, coulomb):
    local = bands.shape[0]
    kernel = coulomb * (1.0 / (NX * NY * NZ))
    own_re = bands[:, 0]
    own_im = bands[:, 1]
    totals = (jnp.zeros_like(own_re), jnp.zeros_like(own_im))
    crossed = lax.ppermute(bands, "band", [(0, 8), (8, 0)])
    gate = None
    for visit_index in range(STEPS):
        if visit_index:
            crossed, _ = lax.optimization_barrier((crossed, gate))
            visitors = crossed + half_tree(crossed, "band")
            own, visitors = lax.optimization_barrier((bands, visitors))
            own_re = own[:, 0]
            own_im = own[:, 1]
        else:
            visitors = own_visitor(bands, "band")
        pair_vis_re = visitors[:, 0]
        pair_vis_im = visitors[:, 1]
        pair_real_part = pair_vis_re[None] * own_re[:, None] + pair_vis_im[None] * own_im[:, None]
        pair_imag_part = pair_vis_re[None] * own_im[:, None] - pair_vis_im[None] * own_re[:, None]
        pair_shape = (local * local,) + pair_real_part.shape[2:]
        real_part = pair_real_part.reshape(pair_shape)
        imag_part = pair_imag_part.reshape(pair_shape)
        potentials_real_part = real_part
        potentials_imag_part = imag_part
        potentials_real_part, potentials_imag_part = transform(
            potentials_real_part, potentials_imag_part, 3, False
        )
        potentials_real_part, potentials_imag_part = transform(
            potentials_real_part, potentials_imag_part, 2, False
        )
        stacked = jnp.stack([potentials_real_part, potentials_imag_part], axis=1)
        gate = stacked
        block = lax.all_to_all(stacked, "grid", split_axis=3, concat_axis=2, tiled=True)
        pencil_real_part, pencil_imag_part = transform(block[:, 0], block[:, 1], 1, False)
        pencil_real_part = pencil_real_part * kernel[None]
        pencil_imag_part = pencil_imag_part * kernel[None]
        pencil_real_part, pencil_imag_part = transform(pencil_real_part, pencil_imag_part, 1, True)
        back = jnp.stack([pencil_real_part, pencil_imag_part], axis=1)
        result = lax.all_to_all(back, "grid", split_axis=2, concat_axis=3, tiled=True)
        potentials_real_part, potentials_imag_part = transform(result[:, 0], result[:, 1], 2, True)
        pot_re, pot_im = transform(potentials_real_part, potentials_imag_part, 3, True)
        accumulate_pot_re = pot_re
        accumulate_pot_im = pot_im
        vis_re = visitors[:, 0][None]
        vis_im = visitors[:, 1][None]
        shape = (local, local) + accumulate_pot_re.shape[1:]
        accumulate_pot_re = accumulate_pot_re.reshape(shape)
        accumulate_pot_im = accumulate_pot_im.reshape(shape)
        add_re = jnp.sum(accumulate_pot_re * vis_re - accumulate_pot_im * vis_im, axis=1)
        add_im = jnp.sum(accumulate_pot_re * vis_im + accumulate_pot_im * vis_re, axis=1)
        totals = (totals[0] + add_re, totals[1] + add_im)
    return -0.25 * jnp.stack([totals[0], totals[1]], axis=1)


def solution(mesh):
    in_specs = (P("band", None, "grid", None, None), P(None, "grid", None))
    out_specs = P("band", None, "grid", None, None)
    return jax.shard_map(body, mesh=mesh, in_specs=in_specs, out_specs=out_specs, check_vma=False)
```

```python
import math

import jax
import jax.numpy as jnp
from jax import lax
from jax.sharding import PartitionSpec as P

NX = 128
NY = 128
NZ = 128
STEPS = 2


einsum_forms = {1: "pnbc,nk->pkbc", 2: "panc,nk->pakc", 3: "pabn,nk->pabk"}


def band_place(half, row, core):
    return half * 8 + row * 2 + core


def half_tree(value, axis):
    def send(operand, pairs):
        return lax.ppermute(operand, axis, [(band_place(h, *a), band_place(h, *b)) for h in (0, 1) for a, b in pairs])

    first = [send(value, [((0, 0), (0, 1))]), send(value, [((0, 0), (1, 0))]), send(value, [((0, 0), (3, 0))])]
    relay = first[1] + first[2]
    second = [
        send(relay, [((1, 0), (1, 1)), ((3, 0), (3, 1))]),
        send(relay, [((1, 0), (2, 0))]),
        send(relay, [((3, 0), (2, 1))]),
    ]
    total = first[0] + relay
    for part in second:
        total = total + part
    return total


def visitors_of(bands, axis):
    index = lax.axis_index(axis)
    head = index % 8 == 0
    own = jnp.where(head, bands, 0).astype(bands.dtype)
    crossed = lax.ppermute(bands, axis, [(0, 8), (8, 0)])
    return [own + half_tree(own, axis), crossed + half_tree(crossed, axis)]


def dft_tables(length):
    indices = jnp.arange(length, dtype=jnp.int32)
    products = indices[:, None] * indices[None, :] % length
    angles = products.astype(jnp.float32) * (2.0 * math.pi / length)
    return (jnp.cos(angles), jnp.sin(angles))


def transform(real_part, imag_part, axis_dim, inverse):
    cosine, sine_table = dft_tables(real_part.shape[axis_dim])
    form = einsum_forms[axis_dim]

    def contract(values, table):
        return jnp.einsum(form, values, table, precision=lax.Precision.HIGH)

    re_cos = contract(real_part, cosine)
    re_sin = contract(real_part, sine_table)
    im_cos = contract(imag_part, cosine)
    im_sin = contract(imag_part, sine_table)
    if inverse:
        return (re_cos - im_sin, im_cos + re_sin)
    return (re_cos + im_sin, im_cos - re_sin)


def body(bands, coulomb):
    local = bands.shape[0]
    kernel = coulomb * (1.0 / (NX * NY * NZ))
    own_re = bands[:, 0]
    own_im = bands[:, 1]
    totals = (jnp.zeros_like(own_re), jnp.zeros_like(own_im))
    for visit_index, visitors in enumerate(visitors_of(bands, "band")):
        if visit_index:
            own, visitors = lax.optimization_barrier((bands, visitors))
            own_re = own[:, 0]
            own_im = own[:, 1]
        pair_vis_re = visitors[:, 0]
        pair_vis_im = visitors[:, 1]
        pair_real_part = pair_vis_re[None] * own_re[:, None] + pair_vis_im[None] * own_im[:, None]
        pair_imag_part = pair_vis_re[None] * own_im[:, None] - pair_vis_im[None] * own_re[:, None]
        pair_shape = (local * local,) + pair_real_part.shape[2:]
        real_part = pair_real_part.reshape(pair_shape)
        imag_part = pair_imag_part.reshape(pair_shape)
        potentials_real_part = real_part
        potentials_imag_part = imag_part
        potentials_real_part, potentials_imag_part = transform(
            potentials_real_part, potentials_imag_part, 3, False
        )
        potentials_real_part, potentials_imag_part = transform(
            potentials_real_part, potentials_imag_part, 2, False
        )
        stacked = jnp.stack([potentials_real_part, potentials_imag_part], axis=1)
        block = lax.all_to_all(stacked, "grid", split_axis=3, concat_axis=2, tiled=True)
        pencil_real_part, pencil_imag_part = transform(block[:, 0], block[:, 1], 1, False)
        pencil_real_part = pencil_real_part * kernel[None]
        pencil_imag_part = pencil_imag_part * kernel[None]
        pencil_real_part, pencil_imag_part = transform(pencil_real_part, pencil_imag_part, 1, True)
        back = jnp.stack([pencil_real_part, pencil_imag_part], axis=1)
        result = lax.all_to_all(back, "grid", split_axis=2, concat_axis=3, tiled=True)
        potentials_real_part, potentials_imag_part = transform(result[:, 0], result[:, 1], 2, True)
        pot_re, pot_im = transform(potentials_real_part, potentials_imag_part, 3, True)
        accumulate_pot_re = pot_re
        accumulate_pot_im = pot_im
        vis_re = visitors[:, 0][None]
        vis_im = visitors[:, 1][None]
        shape = (local, local) + accumulate_pot_re.shape[1:]
        accumulate_pot_re = accumulate_pot_re.reshape(shape)
        accumulate_pot_im = accumulate_pot_im.reshape(shape)
        add_re = jnp.sum(accumulate_pot_re * vis_re - accumulate_pot_im * vis_im, axis=1)
        add_im = jnp.sum(accumulate_pot_re * vis_im + accumulate_pot_im * vis_re, axis=1)
        totals = (totals[0] + add_re, totals[1] + add_im)
    return -0.25 * jnp.stack([totals[0], totals[1]], axis=1)


def solution(mesh):
    in_specs = (P("band", None, "grid", None, None), P(None, "grid", None))
    out_specs = P("band", None, "grid", None, None)
    return jax.shard_map(body, mesh=mesh, in_specs=in_specs, out_specs=out_specs, check_vma=False)
```

```python
import math

import jax
import jax.numpy as jnp
from jax import lax
from jax.sharding import PartitionSpec as P


NX = 128
NY = 128
NZ = 128


einsum_forms = {1: "pnbc,nk->pkbc", 2: "panc,nk->pakc", 3: "pabn,nk->pabk"}


def band_place(half, row, core):
    return half * 8 + row * 2 + core


def half_tree(value, axis):
    def send(operand, pairs):
        return lax.ppermute(operand, axis, [(band_place(h, *a), band_place(h, *b)) for h in (0, 1) for a, b in pairs])

    first = [send(value, [((0, 0), (0, 1))]), send(value, [((0, 0), (1, 0))]), send(value, [((0, 0), (3, 0))])]
    relay = first[1] + first[2]
    second = [
        send(relay, [((1, 0), (1, 1)), ((3, 0), (3, 1))]),
        send(relay, [((1, 0), (2, 0))]),
        send(relay, [((3, 0), (2, 1))]),
    ]
    total = first[0] + relay
    for part in second:
        total = total + part
    return total


def visitors_of(bands, axis):
    index = lax.axis_index(axis)
    head = index % 8 == 0
    own = jnp.where(head, bands, 0).astype(bands.dtype)
    crossed = lax.ppermute(bands, axis, [(0, 8), (8, 0)])
    own = own + half_tree(own, axis)
    crossed = crossed + half_tree(crossed, axis)
    return [own, crossed]


def dft_tables(length):
    indices = jnp.arange(length, dtype=jnp.int32)
    products = indices[:, None] * indices[None, :] % length
    angles = products.astype(jnp.float32) * (2.0 * math.pi / length)
    return (jnp.cos(angles), jnp.sin(angles))


def transform(real_part, imag_part, axis_dim, inverse):
    cosine, sine_table = dft_tables(real_part.shape[axis_dim])
    form = einsum_forms[axis_dim]

    def contract(values, table):
        return jnp.einsum(form, values, table, precision=lax.Precision.HIGH)

    re_cos = contract(real_part, cosine)
    re_sin = contract(real_part, sine_table)
    im_cos = contract(imag_part, cosine)
    im_sin = contract(imag_part, sine_table)
    if inverse:
        return (re_cos - im_sin, im_cos + re_sin)
    return (re_cos + im_sin, im_cos - re_sin)


def body(bands, coulomb):
    local = bands.shape[0]
    kernel = coulomb * (1.0 / (NX * NY * NZ))
    own_re = bands[:, 0]
    own_im = bands[:, 1]
    totals = (jnp.zeros_like(own_re), jnp.zeros_like(own_im))
    for visit_index, visitors in enumerate(visitors_of(bands, "band")):
        if visit_index:
            own, visitors = lax.optimization_barrier((bands, visitors))
            own_re = own[:, 0]
            own_im = own[:, 1]
        pair_vis_re = visitors[:, 0]
        pair_vis_im = visitors[:, 1]
        pair_real_part = pair_vis_re[None] * own_re[:, None] + pair_vis_im[None] * own_im[:, None]
        pair_imag_part = pair_vis_re[None] * own_im[:, None] - pair_vis_im[None] * own_re[:, None]
        pair_shape = (local * local,) + pair_real_part.shape[2:]
        real_part = pair_real_part.reshape(pair_shape)
        imag_part = pair_imag_part.reshape(pair_shape)
        potentials_real_part = real_part
        potentials_imag_part = imag_part
        potentials_real_part, potentials_imag_part = transform(
            potentials_real_part, potentials_imag_part, 3, False
        )
        potentials_real_part, potentials_imag_part = transform(
            potentials_real_part, potentials_imag_part, 2, False
        )
        stacked = jnp.stack([potentials_real_part, potentials_imag_part], axis=1)
        block = lax.all_to_all(stacked, "grid", split_axis=3, concat_axis=2, tiled=True)
        pencil_real_part, pencil_imag_part = transform(block[:, 0], block[:, 1], 1, False)
        pencil_real_part = pencil_real_part * kernel[None]
        pencil_imag_part = pencil_imag_part * kernel[None]
        pencil_real_part, pencil_imag_part = transform(pencil_real_part, pencil_imag_part, 1, True)
        back = jnp.stack([pencil_real_part, pencil_imag_part], axis=1)
        result = lax.all_to_all(back, "grid", split_axis=2, concat_axis=3, tiled=True)
        potentials_real_part, potentials_imag_part = transform(result[:, 0], result[:, 1], 2, True)
        pot_re, pot_im = transform(potentials_real_part, potentials_imag_part, 3, True)
        accumulate_pot_re = pot_re
        accumulate_pot_im = pot_im
        vis_re = visitors[:, 0][None]
        vis_im = visitors[:, 1][None]
        shape = (local, local) + accumulate_pot_re.shape[1:]
        accumulate_pot_re = accumulate_pot_re.reshape(shape)
        accumulate_pot_im = accumulate_pot_im.reshape(shape)
        add_re = jnp.sum(accumulate_pot_re * vis_re - accumulate_pot_im * vis_im, axis=1)
        add_im = jnp.sum(accumulate_pot_re * vis_im + accumulate_pot_im * vis_re, axis=1)
        totals = (totals[0] + add_re, totals[1] + add_im)
    return -0.25 * jnp.stack([totals[0], totals[1]], axis=1)


def solution(mesh):
    in_specs = (P("band", None, "grid", None, None), P(None, "grid", None))
    out_specs = P("band", None, "grid", None, None)
    return jax.shard_map(body, mesh=mesh, in_specs=in_specs, out_specs=out_specs, check_vma=False)
```

```python
import math

import jax
import jax.numpy as jnp
from jax import lax
from jax.sharding import PartitionSpec as P

NX = 128
NY = 128
NZ = 128
STEPS = 2


fused_forms = {1: "prnbc,rntk->ptkbc", 2: "pranc,rntk->ptakc", 3: "prabn,rntk->ptabk"}


def band_place(half, row, core):
    return half * 8 + row * 2 + core


def half_tree(value, axis):
    def send(operand, pairs):
        return lax.ppermute(operand, axis, [(band_place(h, *a), band_place(h, *b)) for h in (0, 1) for a, b in pairs])

    first = [send(value, [((0, 0), (0, 1))]), send(value, [((0, 0), (1, 0))]), send(value, [((0, 0), (3, 0))])]
    relay = first[1] + first[2]
    second = [
        send(relay, [((1, 0), (1, 1)), ((3, 0), (3, 1))]),
        send(relay, [((1, 0), (2, 0))]),
        send(relay, [((3, 0), (2, 1))]),
    ]
    total = first[0] + relay
    for part in second:
        total = total + part
    return total


def visitors_of(bands, axis):
    index = lax.axis_index(axis)
    head = index % 8 == 0
    own = jnp.where(head, bands, 0).astype(bands.dtype)
    crossed = lax.ppermute(bands, axis, [(0, 8), (8, 0)])
    return [own + half_tree(own, axis), crossed + half_tree(crossed, axis)]


def dft_tables(length):
    indices = jnp.arange(length, dtype=jnp.int32)
    products = indices[:, None] * indices[None, :] % length
    angles = products.astype(jnp.float32) * (2.0 * math.pi / length)
    return (jnp.cos(angles), jnp.sin(angles))


def transform(real_part, imag_part, axis_dim, inverse):
    cosine, sine_table = dft_tables(real_part.shape[axis_dim])
    signed = -sine_table if inverse else sine_table
    table = jnp.stack([jnp.stack([cosine, -signed], 1), jnp.stack([signed, cosine], 1)], 0)
    values = jnp.stack([real_part, imag_part], axis=1)
    out = jnp.einsum(fused_forms[axis_dim], values, table, precision=lax.Precision.HIGH)
    return (out[:, 0], out[:, 1])


def body(bands, coulomb):
    local = bands.shape[0]
    kernel = coulomb * (1.0 / (NX * NY * NZ))
    own_re = bands[:, 0]
    own_im = bands[:, 1]
    totals = (jnp.zeros_like(own_re), jnp.zeros_like(own_im))
    for visit_index, visitors in enumerate(visitors_of(bands, "band")):
        if visit_index:
            own, visitors = lax.optimization_barrier((bands, visitors))
            own_re = own[:, 0]
            own_im = own[:, 1]
        pair_vis_re = visitors[:, 0]
        pair_vis_im = visitors[:, 1]
        pair_real_part = pair_vis_re[None] * own_re[:, None] + pair_vis_im[None] * own_im[:, None]
        pair_imag_part = pair_vis_re[None] * own_im[:, None] - pair_vis_im[None] * own_re[:, None]
        pair_shape = (local * local,) + pair_real_part.shape[2:]
        real_part = pair_real_part.reshape(pair_shape)
        imag_part = pair_imag_part.reshape(pair_shape)
        potentials_real_part = real_part
        potentials_imag_part = imag_part
        potentials_real_part, potentials_imag_part = transform(
            potentials_real_part, potentials_imag_part, 3, False
        )
        potentials_real_part, potentials_imag_part = transform(
            potentials_real_part, potentials_imag_part, 2, False
        )
        stacked = jnp.stack([potentials_real_part, potentials_imag_part], axis=1)
        block = lax.all_to_all(stacked, "grid", split_axis=3, concat_axis=2, tiled=True)
        pencil_real_part, pencil_imag_part = transform(block[:, 0], block[:, 1], 1, False)
        pencil_real_part = pencil_real_part * kernel[None]
        pencil_imag_part = pencil_imag_part * kernel[None]
        pencil_real_part, pencil_imag_part = transform(pencil_real_part, pencil_imag_part, 1, True)
        back = jnp.stack([pencil_real_part, pencil_imag_part], axis=1)
        result = lax.all_to_all(back, "grid", split_axis=2, concat_axis=3, tiled=True)
        potentials_real_part, potentials_imag_part = transform(result[:, 0], result[:, 1], 2, True)
        pot_re, pot_im = transform(potentials_real_part, potentials_imag_part, 3, True)
        accumulate_pot_re = pot_re
        accumulate_pot_im = pot_im
        vis_re = visitors[:, 0][None]
        vis_im = visitors[:, 1][None]
        shape = (local, local) + accumulate_pot_re.shape[1:]
        accumulate_pot_re = accumulate_pot_re.reshape(shape)
        accumulate_pot_im = accumulate_pot_im.reshape(shape)
        add_re = jnp.sum(accumulate_pot_re * vis_re - accumulate_pot_im * vis_im, axis=1)
        add_im = jnp.sum(accumulate_pot_re * vis_im + accumulate_pot_im * vis_re, axis=1)
        totals = (totals[0] + add_re, totals[1] + add_im)
    return -0.25 * jnp.stack([totals[0], totals[1]], axis=1)


def solution(mesh):
    in_specs = (P("band", None, "grid", None, None), P(None, "grid", None))
    out_specs = P("band", None, "grid", None, None)
    return jax.shard_map(body, mesh=mesh, in_specs=in_specs, out_specs=out_specs, check_vma=False)
```

```python
import math

import jax
import jax.numpy as jnp
from jax import lax
from jax.sharding import PartitionSpec as P

NX = 128
NY = 128
NZ = 128
STEPS = 2


fused_forms = {1: "prnbc,rntk->ptkbc", 2: "pranc,rntk->ptakc", 3: "prabn,rntk->ptabk"}


def band_place(half, row, core):
    return half * 8 + row * 2 + core


def half_tree(value, axis):
    def send(operand, pairs):
        return lax.ppermute(operand, axis, [(band_place(h, *a), band_place(h, *b)) for h in (0, 1) for a, b in pairs])

    first = [send(value, [((0, 0), (0, 1))]), send(value, [((0, 0), (1, 0))]), send(value, [((0, 0), (3, 0))])]
    relay = first[1] + first[2]
    second = [
        send(relay, [((1, 0), (1, 1)), ((3, 0), (3, 1))]),
        send(relay, [((1, 0), (2, 0))]),
        send(relay, [((3, 0), (2, 1))]),
    ]
    total = first[0] + relay
    for part in second:
        total = total + part
    return total


def visitors_of(bands, axis):
    index = lax.axis_index(axis)
    head = index % 8 == 0
    own = jnp.where(head, bands, 0).astype(bands.dtype)
    crossed = lax.ppermute(bands, axis, [(0, 8), (8, 0)])
    return [own + half_tree(own, axis), crossed + half_tree(crossed, axis)]


def dft_tables(length):
    indices = jnp.arange(length, dtype=jnp.int32)
    products = indices[:, None] * indices[None, :] % length
    angles = products.astype(jnp.float32) * (2.0 * math.pi / length)
    return (jnp.cos(angles), jnp.sin(angles))


def transform(real_part, imag_part, axis_dim, inverse):
    cosine, sine_table = dft_tables(real_part.shape[axis_dim])
    signed = -sine_table if inverse else sine_table
    table = jnp.stack([jnp.stack([cosine, -signed], 1), jnp.stack([signed, cosine], 1)], 0)
    values = jnp.stack([real_part, imag_part], axis=1)
    out = jnp.einsum(fused_forms[axis_dim], values, table, precision=lax.Precision.HIGH)
    return (out[:, 0], out[:, 1])


def body(bands, coulomb):
    local = bands.shape[0]
    kernel = coulomb * (1.0 / (NX * NY * NZ))
    own_re = bands[:, 0]
    own_im = bands[:, 1]
    totals = (jnp.zeros_like(own_re), jnp.zeros_like(own_im))
    for visitors in [jnp.concatenate(visitors_of(bands, "band"), axis=0)]:
        count = visitors.shape[0]
        pair_vis_re = visitors[:, 0]
        pair_vis_im = visitors[:, 1]
        pair_real_part = pair_vis_re[None] * own_re[:, None] + pair_vis_im[None] * own_im[:, None]
        pair_imag_part = pair_vis_re[None] * own_im[:, None] - pair_vis_im[None] * own_re[:, None]
        pair_shape = (local * count,) + pair_real_part.shape[2:]
        real_part = pair_real_part.reshape(pair_shape)
        imag_part = pair_imag_part.reshape(pair_shape)
        potentials_real_part = real_part
        potentials_imag_part = imag_part
        potentials_real_part, potentials_imag_part = transform(
            potentials_real_part, potentials_imag_part, 3, False
        )
        potentials_real_part, potentials_imag_part = transform(
            potentials_real_part, potentials_imag_part, 2, False
        )
        stacked = jnp.stack([potentials_real_part, potentials_imag_part], axis=1)
        block = lax.all_to_all(stacked, "grid", split_axis=3, concat_axis=2, tiled=True)
        pencil_real_part, pencil_imag_part = transform(block[:, 0], block[:, 1], 1, False)
        pencil_real_part = pencil_real_part * kernel[None]
        pencil_imag_part = pencil_imag_part * kernel[None]
        pencil_real_part, pencil_imag_part = transform(pencil_real_part, pencil_imag_part, 1, True)
        back = jnp.stack([pencil_real_part, pencil_imag_part], axis=1)
        result = lax.all_to_all(back, "grid", split_axis=2, concat_axis=3, tiled=True)
        potentials_real_part, potentials_imag_part = transform(result[:, 0], result[:, 1], 2, True)
        pot_re, pot_im = transform(potentials_real_part, potentials_imag_part, 3, True)
        accumulate_pot_re = pot_re
        accumulate_pot_im = pot_im
        vis_re = visitors[:, 0][None]
        vis_im = visitors[:, 1][None]
        shape = (local, count) + accumulate_pot_re.shape[1:]
        accumulate_pot_re = accumulate_pot_re.reshape(shape)
        accumulate_pot_im = accumulate_pot_im.reshape(shape)
        add_re = jnp.sum(accumulate_pot_re * vis_re - accumulate_pot_im * vis_im, axis=1)
        add_im = jnp.sum(accumulate_pot_re * vis_im + accumulate_pot_im * vis_re, axis=1)
        totals = (totals[0] + add_re, totals[1] + add_im)
    return -0.25 * jnp.stack([totals[0], totals[1]], axis=1)


def solution(mesh):
    in_specs = (P("band", None, "grid", None, None), P(None, "grid", None))
    out_specs = P("band", None, "grid", None, None)
    return jax.shard_map(body, mesh=mesh, in_specs=in_specs, out_specs=out_specs, check_vma=False)
```

```python
import math

import jax
import jax.numpy as jnp
from jax import lax
from jax.sharding import PartitionSpec as P

NX = 128
NY = 128
NZ = 128
STEPS = 2


fused_forms = {1: "prnbc,rntk->ptkbc", 2: "pranc,rntk->ptakc", 3: "prabn,rntk->ptabk"}


def band_place(half, row, core):
    return half * 8 + row * 2 + core


def send(operand, axis, pairs):
    return lax.ppermute(operand, axis, [(band_place(h, *a), band_place(h, *b)) for h in (0, 1) for a, b in pairs])


def visitors_of(bands, axis):
    place = lax.axis_index(axis) % 8

    def at(*places):
        hit = place == places[0]
        for other in places[1:]:
            hit = hit | (place == other)
        return hit

    own_head = jnp.where(at(0), bands, 0).astype(bands.dtype)
    crossed_head = lax.ppermute(bands, axis, [(0, 8), (8, 0)])
    first = [send(own_head, axis, [((0, 0), pair)]) for pair in ((0, 1), (1, 0), (3, 0))]
    relay = first[1] + first[2]
    mixed = relay + crossed_head
    q1 = send(mixed, axis, [((1, 0), (1, 1)), ((3, 0), (3, 1)), ((0, 0), (0, 1))])
    q2 = send(mixed, axis, [((1, 0), (2, 0)), ((0, 0), (1, 0))])
    q3 = send(mixed, axis, [((3, 0), (2, 1)), ((0, 0), (3, 0))])
    zero = jnp.zeros_like(bands)
    own = own_head + first[0] + relay + jnp.where(at(3, 7), q1, zero) + jnp.where(at(4), q2, zero)
    own = own + jnp.where(at(5), q3, zero)
    crossed_relay = jnp.where(at(2), q2, zero) + jnp.where(at(6), q3, zero)
    third_a = send(crossed_relay, axis, [((1, 0), (1, 1)), ((3, 0), (2, 1))])
    third_b = send(crossed_relay, axis, [((1, 0), (2, 0)), ((3, 0), (3, 1))])
    crossed = crossed_head + jnp.where(at(1), q1, zero) + crossed_relay + third_a + third_b
    return [own, crossed]


def dft_tables(length):
    indices = jnp.arange(length, dtype=jnp.int32)
    products = indices[:, None] * indices[None, :] % length
    angles = products.astype(jnp.float32) * (2.0 * math.pi / length)
    return (jnp.cos(angles), jnp.sin(angles))


def transform(real_part, imag_part, axis_dim, inverse):
    cosine, sine_table = dft_tables(real_part.shape[axis_dim])
    signed = -sine_table if inverse else sine_table
    table = jnp.stack([jnp.stack([cosine, -signed], 1), jnp.stack([signed, cosine], 1)], 0)
    values = jnp.stack([real_part, imag_part], axis=1)
    out = jnp.einsum(fused_forms[axis_dim], values, table, precision=lax.Precision.HIGH)
    return (out[:, 0], out[:, 1])


def body(bands, coulomb):
    local = bands.shape[0]
    kernel = coulomb * (1.0 / (NX * NY * NZ))
    own_re = bands[:, 0]
    own_im = bands[:, 1]
    totals = (jnp.zeros_like(own_re), jnp.zeros_like(own_im))
    for visit_index, visitors in enumerate(visitors_of(bands, "band")):
        if visit_index:
            own, visitors = lax.optimization_barrier((bands, visitors))
            own_re = own[:, 0]
            own_im = own[:, 1]
        pair_vis_re = visitors[:, 0]
        pair_vis_im = visitors[:, 1]
        pair_real_part = pair_vis_re[None] * own_re[:, None] + pair_vis_im[None] * own_im[:, None]
        pair_imag_part = pair_vis_re[None] * own_im[:, None] - pair_vis_im[None] * own_re[:, None]
        pair_shape = (local * local,) + pair_real_part.shape[2:]
        real_part = pair_real_part.reshape(pair_shape)
        imag_part = pair_imag_part.reshape(pair_shape)
        potentials_real_part = real_part
        potentials_imag_part = imag_part
        potentials_real_part, potentials_imag_part = transform(
            potentials_real_part, potentials_imag_part, 3, False
        )
        potentials_real_part, potentials_imag_part = transform(
            potentials_real_part, potentials_imag_part, 2, False
        )
        stacked = jnp.stack([potentials_real_part, potentials_imag_part], axis=1)
        block = lax.all_to_all(stacked, "grid", split_axis=3, concat_axis=2, tiled=True)
        pencil_real_part, pencil_imag_part = transform(block[:, 0], block[:, 1], 1, False)
        pencil_real_part = pencil_real_part * kernel[None]
        pencil_imag_part = pencil_imag_part * kernel[None]
        pencil_real_part, pencil_imag_part = transform(pencil_real_part, pencil_imag_part, 1, True)
        back = jnp.stack([pencil_real_part, pencil_imag_part], axis=1)
        result = lax.all_to_all(back, "grid", split_axis=2, concat_axis=3, tiled=True)
        potentials_real_part, potentials_imag_part = transform(result[:, 0], result[:, 1], 2, True)
        pot_re, pot_im = transform(potentials_real_part, potentials_imag_part, 3, True)
        accumulate_pot_re = pot_re
        accumulate_pot_im = pot_im
        vis_re = visitors[:, 0][None]
        vis_im = visitors[:, 1][None]
        shape = (local, local) + accumulate_pot_re.shape[1:]
        accumulate_pot_re = accumulate_pot_re.reshape(shape)
        accumulate_pot_im = accumulate_pot_im.reshape(shape)
        add_re = jnp.sum(accumulate_pot_re * vis_re - accumulate_pot_im * vis_im, axis=1)
        add_im = jnp.sum(accumulate_pot_re * vis_im + accumulate_pot_im * vis_re, axis=1)
        totals = (totals[0] + add_re, totals[1] + add_im)
    return -0.25 * jnp.stack([totals[0], totals[1]], axis=1)


def solution(mesh):
    in_specs = (P("band", None, "grid", None, None), P(None, "grid", None))
    out_specs = P("band", None, "grid", None, None)
    return jax.shard_map(body, mesh=mesh, in_specs=in_specs, out_specs=out_specs, check_vma=False)
```

```python
import math

import jax
import jax.numpy as jnp
from jax import lax
from jax.sharding import PartitionSpec as P


NX = 128
NY = 128
NZ = 128


fused_forms = {1: "prnbc,rntk->ptkbc", 2: "pranc,rntk->ptakc", 3: "prabn,rntk->ptabk"}


def band_place(half, row, core):
    return half * 8 + row * 2 + core


def half_tree(value, axis):
    def send(operand, pairs):
        return lax.ppermute(operand, axis, [(band_place(h, *a), band_place(h, *b)) for h in (0, 1) for a, b in pairs])

    first = [send(value, [((0, 0), (0, 1))]), send(value, [((0, 0), (1, 0))]), send(value, [((0, 0), (3, 0))])]
    relay = first[1] + first[2]
    second = [
        send(relay, [((1, 0), (1, 1)), ((3, 0), (3, 1))]),
        send(relay, [((1, 0), (2, 0))]),
        send(relay, [((3, 0), (2, 1))]),
    ]
    total = first[0] + relay
    for part in second:
        total = total + part
    return total


def visitors_of(bands, axis):
    index = lax.axis_index(axis)
    head = index % 8 == 0
    own = jnp.where(head, bands, 0).astype(bands.dtype)
    crossed = lax.ppermute(bands, axis, [(0, 8), (8, 0)])
    own = own + half_tree(own, axis)
    crossed = crossed + half_tree(crossed, axis)
    return [own, crossed]


def dft_tables(length):
    indices = jnp.arange(length, dtype=jnp.int32)
    products = indices[:, None] * indices[None, :] % length
    angles = products.astype(jnp.float32) * (2.0 * math.pi / length)
    return (jnp.cos(angles), jnp.sin(angles))


def transform(real_part, imag_part, axis_dim, inverse):
    cosine, sine_table = dft_tables(real_part.shape[axis_dim])
    signed = -sine_table if inverse else sine_table
    table = jnp.stack([jnp.stack([cosine, -signed], 1), jnp.stack([signed, cosine], 1)], 0)
    values = jnp.stack([real_part, imag_part], axis=1)
    out = jnp.einsum(fused_forms[axis_dim], values, table, precision=lax.Precision.HIGH)
    return (out[:, 0], out[:, 1])


def body(bands, coulomb):
    local = bands.shape[0]
    kernel = coulomb * (1.0 / (NX * NY * NZ))
    own_re = bands[:, 0]
    own_im = bands[:, 1]
    totals = (jnp.zeros_like(own_re), jnp.zeros_like(own_im))
    for visit_index, visitors in enumerate(visitors_of(bands, "band")):
        if visit_index:
            own, visitors = lax.optimization_barrier((bands, visitors))
            own_re = own[:, 0]
            own_im = own[:, 1]
        pair_vis_re = visitors[:, 0]
        pair_vis_im = visitors[:, 1]
        pair_real_part = pair_vis_re[None] * own_re[:, None] + pair_vis_im[None] * own_im[:, None]
        pair_imag_part = pair_vis_re[None] * own_im[:, None] - pair_vis_im[None] * own_re[:, None]
        pair_shape = (local * local,) + pair_real_part.shape[2:]
        real_part = pair_real_part.reshape(pair_shape)
        imag_part = pair_imag_part.reshape(pair_shape)
        potentials_real_part = real_part
        potentials_imag_part = imag_part
        potentials_real_part, potentials_imag_part = transform(
            potentials_real_part, potentials_imag_part, 3, False
        )
        potentials_real_part, potentials_imag_part = transform(
            potentials_real_part, potentials_imag_part, 2, False
        )
        stacked = jnp.stack([potentials_real_part, potentials_imag_part], axis=1)
        block = lax.all_to_all(stacked, "grid", split_axis=3, concat_axis=2, tiled=True)
        pencil_real_part, pencil_imag_part = transform(block[:, 0], block[:, 1], 1, False)
        pencil_real_part = pencil_real_part * kernel[None]
        pencil_imag_part = pencil_imag_part * kernel[None]
        pencil_real_part, pencil_imag_part = transform(pencil_real_part, pencil_imag_part, 1, True)
        back = jnp.stack([pencil_real_part, pencil_imag_part], axis=1)
        result = lax.all_to_all(back, "grid", split_axis=2, concat_axis=3, tiled=True)
        potentials_real_part, potentials_imag_part = transform(result[:, 0], result[:, 1], 2, True)
        pot_re, pot_im = transform(potentials_real_part, potentials_imag_part, 3, True)
        accumulate_pot_re = pot_re
        accumulate_pot_im = pot_im
        vis_re = visitors[:, 0][None]
        vis_im = visitors[:, 1][None]
        shape = (local, local) + accumulate_pot_re.shape[1:]
        accumulate_pot_re = accumulate_pot_re.reshape(shape)
        accumulate_pot_im = accumulate_pot_im.reshape(shape)
        add_re = jnp.sum(accumulate_pot_re * vis_re - accumulate_pot_im * vis_im, axis=1)
        add_im = jnp.sum(accumulate_pot_re * vis_im + accumulate_pot_im * vis_re, axis=1)
        totals = (totals[0] + add_re, totals[1] + add_im)
    return -0.25 * jnp.stack([totals[0], totals[1]], axis=1)


def solution(mesh):
    in_specs = (P("band", None, "grid", None, None), P(None, "grid", None))
    out_specs = P("band", None, "grid", None, None)
    return jax.shard_map(body, mesh=mesh, in_specs=in_specs, out_specs=out_specs, check_vma=False)
```

```python
import math

import jax
import jax.numpy as jnp
from jax import lax
from jax.sharding import PartitionSpec as P

NX = 128
NY = 128
NZ = 128
STEPS = 2


fused_forms = {1: "prnbc,rntk->ptkbc", 2: "pranc,rntk->ptakc", 3: "prabn,rntk->ptabk"}


def band_place(half, row, core):
    return half * 8 + row * 2 + core


def half_tree(value, axis, roots=(0, 0)):
    def send(operand, pairs):
        return lax.ppermute(
            operand,
            axis,
            [
                (band_place(h, (a[0] + roots[h]) % 4, a[1]), band_place(h, (b[0] + roots[h]) % 4, b[1]))
                for h in (0, 1)
                for a, b in pairs
            ],
        )

    first = [send(value, [((0, 0), (0, 1))]), send(value, [((0, 0), (1, 0))]), send(value, [((0, 0), (3, 0))])]
    relay = first[1] + first[2]
    second = [
        send(relay, [((1, 0), (1, 1)), ((3, 0), (3, 1))]),
        send(relay, [((1, 0), (2, 0))]),
        send(relay, [((3, 0), (2, 1))]),
    ]
    total = first[0] + relay
    for part in second:
        total = total + part
    return total


def visitors_of(bands, axis):
    index = lax.axis_index(axis)
    head = index % 8 == 0
    own = jnp.where(head, bands, 0).astype(bands.dtype)
    crossed = lax.ppermute(bands, axis, [(band_place(0, 0, 0), band_place(1, 1, 0)), (band_place(1, 0, 0), band_place(0, 3, 0))])
    return [own + half_tree(own, axis), crossed + half_tree(crossed, axis, roots=(3, 1))]


def dft_tables(length):
    indices = jnp.arange(length, dtype=jnp.int32)
    products = indices[:, None] * indices[None, :] % length
    angles = products.astype(jnp.float32) * (2.0 * math.pi / length)
    return (jnp.cos(angles), jnp.sin(angles))


def transform(real_part, imag_part, axis_dim, inverse):
    cosine, sine_table = dft_tables(real_part.shape[axis_dim])
    signed = -sine_table if inverse else sine_table
    table = jnp.stack([jnp.stack([cosine, -signed], 1), jnp.stack([signed, cosine], 1)], 0)
    values = jnp.stack([real_part, imag_part], axis=1)
    out = jnp.einsum(fused_forms[axis_dim], values, table, precision=lax.Precision.HIGH)
    return (out[:, 0], out[:, 1])


def body(bands, coulomb):
    local = bands.shape[0]
    kernel = coulomb * (1.0 / (NX * NY * NZ))
    own_re = bands[:, 0]
    own_im = bands[:, 1]
    totals = (jnp.zeros_like(own_re), jnp.zeros_like(own_im))
    for visit_index, visitors in enumerate(visitors_of(bands, "band")):
        if visit_index:
            own, visitors = lax.optimization_barrier((bands, visitors))
            own_re = own[:, 0]
            own_im = own[:, 1]
        pair_vis_re = visitors[:, 0]
        pair_vis_im = visitors[:, 1]
        pair_real_part = pair_vis_re[None] * own_re[:, None] + pair_vis_im[None] * own_im[:, None]
        pair_imag_part = pair_vis_re[None] * own_im[:, None] - pair_vis_im[None] * own_re[:, None]
        pair_shape = (local * local,) + pair_real_part.shape[2:]
        real_part = pair_real_part.reshape(pair_shape)
        imag_part = pair_imag_part.reshape(pair_shape)
        potentials_real_part = real_part
        potentials_imag_part = imag_part
        potentials_real_part, potentials_imag_part = transform(
            potentials_real_part, potentials_imag_part, 3, False
        )
        potentials_real_part, potentials_imag_part = transform(
            potentials_real_part, potentials_imag_part, 2, False
        )
        stacked = jnp.stack([potentials_real_part, potentials_imag_part], axis=1)
        block = lax.all_to_all(stacked, "grid", split_axis=3, concat_axis=2, tiled=True)
        pencil_real_part, pencil_imag_part = transform(block[:, 0], block[:, 1], 1, False)
        pencil_real_part = pencil_real_part * kernel[None]
        pencil_imag_part = pencil_imag_part * kernel[None]
        pencil_real_part, pencil_imag_part = transform(pencil_real_part, pencil_imag_part, 1, True)
        back = jnp.stack([pencil_real_part, pencil_imag_part], axis=1)
        result = lax.all_to_all(back, "grid", split_axis=2, concat_axis=3, tiled=True)
        potentials_real_part, potentials_imag_part = transform(result[:, 0], result[:, 1], 2, True)
        pot_re, pot_im = transform(potentials_real_part, potentials_imag_part, 3, True)
        accumulate_pot_re = pot_re
        accumulate_pot_im = pot_im
        vis_re = visitors[:, 0][None]
        vis_im = visitors[:, 1][None]
        shape = (local, local) + accumulate_pot_re.shape[1:]
        accumulate_pot_re = accumulate_pot_re.reshape(shape)
        accumulate_pot_im = accumulate_pot_im.reshape(shape)
        add_re = jnp.sum(accumulate_pot_re * vis_re - accumulate_pot_im * vis_im, axis=1)
        add_im = jnp.sum(accumulate_pot_re * vis_im + accumulate_pot_im * vis_re, axis=1)
        totals = (totals[0] + add_re, totals[1] + add_im)
    return -0.25 * jnp.stack([totals[0], totals[1]], axis=1)


def solution(mesh):
    in_specs = (P("band", None, "grid", None, None), P(None, "grid", None))
    out_specs = P("band", None, "grid", None, None)
    return jax.shard_map(body, mesh=mesh, in_specs=in_specs, out_specs=out_specs, check_vma=False)
```

```python
import math

import jax
import jax.numpy as jnp
from jax import lax
from jax.sharding import PartitionSpec as P


NX = 128
NY = 128
NZ = 128


fused_forms = {1: "prnbc,rntk->ptkbc", 2: "pranc,rntk->ptakc", 3: "prabn,rntk->ptabk"}


def band_place(half, row, core):
    return half * 8 + row * 2 + core


def half_tree(value, axis):
    def send(operand, pairs):
        return lax.ppermute(operand, axis, [(band_place(h, *a), band_place(h, *b)) for h in (0, 1) for a, b in pairs])

    first = [send(value, [((0, 0), (1, 0))]), send(value, [((0, 0), (3, 0))]), send(value, [((0, 0), (0, 1))])]
    relay = first[0] + first[1]
    second = [
        send(relay, [((1, 0), (2, 0))]),
        send(relay, [((3, 0), (2, 1))]),
        send(relay, [((1, 0), (1, 1)), ((3, 0), (3, 1))]),
    ]
    total = first[2] + relay
    for part in second:
        total = total + part
    return total


def visitors_of(bands, axis):
    index = lax.axis_index(axis)
    head = index % 8 == 0
    own = jnp.where(head, bands, 0).astype(bands.dtype)
    crossed = lax.ppermute(bands, axis, [(0, 8), (8, 0)])
    return [own + half_tree(own, axis), crossed + half_tree(crossed, axis)]


def dft_tables(length):
    indices = jnp.arange(length, dtype=jnp.int32)
    products = indices[:, None] * indices[None, :] % length
    angles = products.astype(jnp.float32) * (2.0 * math.pi / length)
    return (jnp.cos(angles), jnp.sin(angles))


def transform(real_part, imag_part, axis_dim, inverse):
    cosine, sine_table = dft_tables(real_part.shape[axis_dim])
    signed = -sine_table if inverse else sine_table
    table = jnp.stack([jnp.stack([cosine, -signed], 1), jnp.stack([signed, cosine], 1)], 0)
    values = jnp.stack([real_part, imag_part], axis=1)
    out = jnp.einsum(fused_forms[axis_dim], values, table, precision=lax.Precision.HIGH)
    return (out[:, 0], out[:, 1])


def body(bands, coulomb):
    local = bands.shape[0]
    kernel = coulomb * (1.0 / (NX * NY * NZ))
    own_re = bands[:, 0]
    own_im = bands[:, 1]
    totals = (jnp.zeros_like(own_re), jnp.zeros_like(own_im))
    for visit_index, visitors in enumerate(visitors_of(bands, "band")):
        if visit_index:
            own, visitors = lax.optimization_barrier((bands, visitors))
            own_re = own[:, 0]
            own_im = own[:, 1]
        pair_vis_re = visitors[:, 0]
        pair_vis_im = visitors[:, 1]
        pair_real_part = pair_vis_re[None] * own_re[:, None] + pair_vis_im[None] * own_im[:, None]
        pair_imag_part = pair_vis_re[None] * own_im[:, None] - pair_vis_im[None] * own_re[:, None]
        pair_shape = (local * local,) + pair_real_part.shape[2:]
        real_part = pair_real_part.reshape(pair_shape)
        imag_part = pair_imag_part.reshape(pair_shape)
        potentials_real_part = real_part
        potentials_imag_part = imag_part
        potentials_real_part, potentials_imag_part = transform(
            potentials_real_part, potentials_imag_part, 3, False
        )
        potentials_real_part, potentials_imag_part = transform(
            potentials_real_part, potentials_imag_part, 2, False
        )
        stacked = jnp.stack([potentials_real_part, potentials_imag_part], axis=1)
        block = lax.all_to_all(stacked, "grid", split_axis=3, concat_axis=2, tiled=True)
        pencil_real_part, pencil_imag_part = transform(block[:, 0], block[:, 1], 1, False)
        pencil_real_part = pencil_real_part * kernel[None]
        pencil_imag_part = pencil_imag_part * kernel[None]
        pencil_real_part, pencil_imag_part = transform(pencil_real_part, pencil_imag_part, 1, True)
        back = jnp.stack([pencil_real_part, pencil_imag_part], axis=1)
        result = lax.all_to_all(back, "grid", split_axis=2, concat_axis=3, tiled=True)
        potentials_real_part, potentials_imag_part = transform(result[:, 0], result[:, 1], 2, True)
        pot_re, pot_im = transform(potentials_real_part, potentials_imag_part, 3, True)
        accumulate_pot_re = pot_re
        accumulate_pot_im = pot_im
        vis_re = visitors[:, 0][None]
        vis_im = visitors[:, 1][None]
        shape = (local, local) + accumulate_pot_re.shape[1:]
        accumulate_pot_re = accumulate_pot_re.reshape(shape)
        accumulate_pot_im = accumulate_pot_im.reshape(shape)
        add_re = jnp.sum(accumulate_pot_re * vis_re - accumulate_pot_im * vis_im, axis=1)
        add_im = jnp.sum(accumulate_pot_re * vis_im + accumulate_pot_im * vis_re, axis=1)
        totals = (totals[0] + add_re, totals[1] + add_im)
    return -0.25 * jnp.stack([totals[0], totals[1]], axis=1)


def solution(mesh):
    in_specs = (P("band", None, "grid", None, None), P(None, "grid", None))
    out_specs = P("band", None, "grid", None, None)
    return jax.shard_map(body, mesh=mesh, in_specs=in_specs, out_specs=out_specs, check_vma=False)
```

```python
import math

import jax
import jax.numpy as jnp
from jax import lax
from jax.sharding import PartitionSpec as P


NX = 128
NY = 128
NZ = 128


fused_forms = {1: "prnbc,rntk->ptkbc", 2: "pranc,rntk->ptakc", 3: "prabn,rntk->ptabk"}


def band_place(half, row, core):
    return half * 8 + row * 2 + core


def half_tree(value, axis):
    def send(operand, pairs):
        return lax.ppermute(operand, axis, [(band_place(h, *a), band_place(h, *b)) for h in (0, 1) for a, b in pairs])

    first = [send(value, [((0, 0), (0, 1))]), send(value, [((0, 0), (1, 0))]), send(value, [((0, 0), (3, 0))])]
    relay = first[1] + first[2]
    second = [
        send(relay, [((1, 0), (1, 1)), ((3, 0), (3, 1))]),
        send(relay, [((1, 0), (2, 0))]),
        send(relay, [((3, 0), (2, 1))]),
    ]
    total = first[0] + relay
    for part in second:
        total = total + part
    return total


def visitors_of(bands, axis):
    index = lax.axis_index(axis)
    head = index % 8 == 0
    own = jnp.where(head, bands, 0).astype(bands.dtype)
    crossed = lax.ppermute(bands, axis, [(0, 8), (8, 0)])
    return [own + half_tree(own, axis), crossed + half_tree(crossed, axis)]


def dft_tables(length):
    indices = jnp.arange(length, dtype=jnp.int32)
    products = indices[:, None] * indices[None, :] % length
    angles = products.astype(jnp.float32) * (2.0 * math.pi / length)
    return (jnp.cos(angles), jnp.sin(angles))


def transform(real_part, imag_part, axis_dim, inverse):
    cosine, sine_table = dft_tables(real_part.shape[axis_dim])
    signed = -sine_table if inverse else sine_table
    table = jnp.stack([jnp.stack([cosine, -signed], 1), jnp.stack([signed, cosine], 1)], 0)
    values = jnp.stack([real_part, imag_part], axis=1)
    out = jnp.einsum(fused_forms[axis_dim], values, table, precision=lax.Precision.HIGH)
    return (out[:, 0], out[:, 1])


def body(bands, coulomb):
    local = bands.shape[0]
    kernel = coulomb * (-0.25 / (NX * NY * NZ))
    own_re = bands[:, 0]
    own_im = bands[:, 1]
    totals = (jnp.zeros_like(own_re), jnp.zeros_like(own_im))
    for visit_index, visitors in enumerate(visitors_of(bands, "band")):
        if visit_index:
            own, visitors = lax.optimization_barrier((bands, visitors))
            own_re = own[:, 0]
            own_im = own[:, 1]
        pair_vis_re = visitors[:, 0]
        pair_vis_im = visitors[:, 1]
        pair_real_part = pair_vis_re[None] * own_re[:, None] + pair_vis_im[None] * own_im[:, None]
        pair_imag_part = pair_vis_re[None] * own_im[:, None] - pair_vis_im[None] * own_re[:, None]
        pair_shape = (local * local,) + pair_real_part.shape[2:]
        real_part = pair_real_part.reshape(pair_shape)
        imag_part = pair_imag_part.reshape(pair_shape)
        potentials_real_part = real_part
        potentials_imag_part = imag_part
        potentials_real_part, potentials_imag_part = transform(
            potentials_real_part, potentials_imag_part, 3, False
        )
        potentials_real_part, potentials_imag_part = transform(
            potentials_real_part, potentials_imag_part, 2, False
        )
        stacked = jnp.stack([potentials_real_part, potentials_imag_part], axis=1)
        block = lax.all_to_all(stacked, "grid", split_axis=3, concat_axis=2, tiled=True)
        pencil_real_part, pencil_imag_part = transform(block[:, 0], block[:, 1], 1, False)
        pair_kernel, _ = lax.optimization_barrier((kernel, block))
        pencil_real_part = pencil_real_part * pair_kernel[None]
        pencil_imag_part = pencil_imag_part * pair_kernel[None]
        pencil_real_part, pencil_imag_part = transform(pencil_real_part, pencil_imag_part, 1, True)
        back = jnp.stack([pencil_real_part, pencil_imag_part], axis=1)
        result = lax.all_to_all(back, "grid", split_axis=2, concat_axis=3, tiled=True)
        potentials_real_part, potentials_imag_part = transform(result[:, 0], result[:, 1], 2, True)
        pot_re, pot_im = transform(potentials_real_part, potentials_imag_part, 3, True)
        accumulate_pot_re = pot_re
        accumulate_pot_im = pot_im
        vis_re = visitors[:, 0][None]
        vis_im = visitors[:, 1][None]
        shape = (local, local) + accumulate_pot_re.shape[1:]
        accumulate_pot_re = accumulate_pot_re.reshape(shape)
        accumulate_pot_im = accumulate_pot_im.reshape(shape)
        add_re = jnp.sum(accumulate_pot_re * vis_re - accumulate_pot_im * vis_im, axis=1)
        add_im = jnp.sum(accumulate_pot_re * vis_im + accumulate_pot_im * vis_re, axis=1)
        totals = (totals[0] + add_re, totals[1] + add_im)
    return jnp.stack([totals[0], totals[1]], axis=1)


def solution(mesh):
    in_specs = (P("band", None, "grid", None, None), P(None, "grid", None))
    out_specs = P("band", None, "grid", None, None)
    return jax.shard_map(body, mesh=mesh, in_specs=in_specs, out_specs=out_specs, check_vma=False)
```
